512 devices in a mesh: outer: 32 (over z, x_hi), inner: 16 (over x_lo, y, core).
Axes of the slice: x: 4 (x_hi: 2, x_lo: 2; x = x_hi * 2 + x_lo), y: 4, z: 16, core: 2. Of those that a mesh axis runs over, the one named last changes fastest.
Arguments:
- queries: bfloat16 [16384, 128], P('inner'), may hold values from -150 to 150
- key_rows: bfloat16 [131072, 128], P(('outer', 'inner')), may hold values from -4.5 to 4.5
- value_rows: bfloat16 [131072, 128], P(('outer', 'inner')), may hold values from -6 to 6
Outputs:
- attended: bfloat16 [16384, 128], P('inner')
The draws below stay inside these ranges and needn't reach their ends.
All inputs are finite; a program needn't handle non-finite values.
Results may differ from the reference program's by a relative error of at most 0.015.
Values may be sent and summed in bfloat16 or wider, within the bound.
No kernel may reach another device: no remote copies, remote signals or barrier semaphores. Data moves between devices by JAX's collectives and lax.ppermute only.
A program may use at most 64 MiB of HBM per device.

```python
import math
import jax
import jax.numpy as jnp
from jax import lax

HD = 128
QUERIES = 16384
KEYS = 131072


def draw_queries(key, part):
    limit = float(min(300, 16384 // HD + 22))
    spread = jnp.exp(jax.random.uniform(jax.random.fold_in(key, 9), (QUERIES, 1), jnp.float32, math.log(3.5), math.log(40.0)))
    entries = jnp.clip(spread * jax.random.normal(jax.random.fold_in(key, 5), (QUERIES, HD), jnp.float32), -limit, limit)
    return entries.astype(jnp.bfloat16)


def draw_key_rows(key, part):
    entries = jnp.clip(jax.random.normal(jax.random.fold_in(key, 7), (KEYS, HD), jnp.float32), -4.5, 4.5)
    return entries.astype(jnp.bfloat16)


def steps_of(key, shape, split, least, high):
    gain = 1.0
    for axis_at, shards_of in split:
        draws = jax.random.uniform(jax.random.fold_in(jax.random.fold_in(key, 6), axis_at), (shards_of,), jnp.float32, least / len(split), high / len(split))
        gain = gain * jnp.repeat(jnp.exp(draws), shape[axis_at] // shards_of).reshape((-1,) + (1,) * (len(shape) - 1 - axis_at))
    return gain


def normal_values(own_key, extent, width, most, pieces=(), dtype=jnp.bfloat16):
    gain = steps_of(own_key, extent, pieces, -0.22, 0.18) if pieces else 1.0
    result = jax.random.normal(own_key, extent, jnp.float32) * width * gain
    return jnp.minimum(jnp.maximum(result, -most), most).astype(dtype)


def setup_inputs(seed: int = 0) -> dict:
    arg_keys = jax.random.split(jax.random.key(seed), 4)
    queries = draw_queries(jax.random.fold_in(arg_keys[3], 71), 0)
    key_rows = draw_key_rows(jax.random.fold_in(arg_keys[3], 71), 0)
    value_rows = normal_values(arg_keys[2], (KEYS, HD), 1.0, 6.0, ((0, 512),))
    return {"queries": queries, "key_rows": key_rows, "value_rows": value_rows}


def reference(queries, key_rows, value_rows):
    score_scale = 1.0 / math.sqrt(HD)
    block_rows = math.gcd(QUERIES, 256)

    def attend_block(query_block):
        scores = jnp.dot(query_block, key_rows.T, preferred_element_type=jnp.float32) * score_scale
        row_peak = lax.optimization_barrier(jnp.max(scores, axis=1))
        probs = jnp.exp(scores - row_peak[:, None])
        row_total = lax.optimization_barrier(jnp.sum(probs, axis=1))
        numerator = jnp.dot(probs.astype(jnp.bfloat16), value_rows, preferred_element_type=jnp.float32)
        return (numerator / row_total[:, None]).astype(jnp.bfloat16)
    blocks = queries.reshape(QUERIES // block_rows, block_rows, HD)
    return lax.map(attend_block, blocks).reshape(QUERIES, HD)
```

```python
import functools
import math

import jax
import jax.numpy as jnp
from jax import lax
from jax.experimental import pallas as pl
from jax.experimental.pallas import tpu as pltpu
from jax.sharding import PartitionSpec as P


def attend_kernel(scale, q_ref, k_ref, v_ref, s_ref, m_ref, l_ref, acc, m_s, l_s):
    step = pl.program_id(1)

    @pl.when(step == 0)
    def _():
        acc[...] = jnp.zeros_like(acc)
        m_s[...] = jnp.full_like(m_s, -1e30)
        l_s[...] = jnp.zeros_like(l_s)

    scores = (
        lax.dot_general(
            q_ref[...], k_ref[...], (((1,), (1,)), ((), ())), preferred_element_type=jnp.float32
        )
        * scale
    )
    m_prev = m_s[...]
    m_new = jnp.maximum(m_prev, jnp.max(scores, axis=1, keepdims=True))
    rescale = jnp.exp(m_prev - m_new)
    probs = jnp.exp(scores - m_new)
    l_s[...] = l_s[...] * rescale + jnp.sum(probs, axis=1, keepdims=True)
    acc[...] = acc[...] * rescale + jnp.dot(
        probs.astype(jnp.bfloat16), v_ref[...], preferred_element_type=jnp.float32
    )
    m_s[...] = m_new

    @pl.when(step == pl.num_programs(1) - 1)
    def _():
        s_ref[...] = acc[...]
        m_ref[...] = m_s[...]
        l_ref[...] = l_s[...]


def local_partial(queries, kv, tq=512, tk=512):
    rows, head = queries.shape
    keys = kv.shape[0]
    scale = 1.0 / math.sqrt(head)
    grid = (rows // tq, keys // tk)
    return pl.pallas_call(
        functools.partial(attend_kernel, scale),
        grid=grid,
        in_specs=[
            pl.BlockSpec((tq, head), lambda i, j: (i, 0)),
            pl.BlockSpec((tk, head), lambda i, j: (j, 0)),
            pl.BlockSpec((tk, head), lambda i, j: (j, 1)),
        ],
        out_specs=[
            pl.BlockSpec((tq, head), lambda i, j: (i, 0)),
            pl.BlockSpec((tq, 1), lambda i, j: (i, 0)),
            pl.BlockSpec((tq, 1), lambda i, j: (i, 0)),
        ],
        out_shape=[
            jax.ShapeDtypeStruct((rows, head), jnp.float32),
            jax.ShapeDtypeStruct((rows, 1), jnp.float32),
            jax.ShapeDtypeStruct((rows, 1), jnp.float32),
        ],
        scratch_shapes=[
            pltpu.VMEM((tq, head), jnp.float32),
            pltpu.VMEM((tq, 1), jnp.float32),
            pltpu.VMEM((tq, 1), jnp.float32),
        ],
        compiler_params=pltpu.CompilerParams(dimension_semantics=("parallel", "arbitrary")),
        cost_estimate=pl.CostEstimate(
            flops=4 * rows * keys * head,
            transcendentals=rows * keys,
            bytes_accessed=rows * head * 6 + keys * head * 4 * grid[0],
        ),
    )(queries, kv, kv)


def on_device(queries, key_rows, value_rows):
    rows, head = queries.shape
    kv = lax.all_gather(jnp.concatenate([key_rows, value_rows], axis=1), "inner", axis=0, tiled=True)
    part_sum, part_peak, part_total = local_partial(queries, kv)

    ranges = lax.axis_size("outer")
    packed = jnp.concatenate([part_sum, part_peak, part_total], axis=1)
    got = lax.all_to_all(packed, "outer", 0, 0, tiled=True)
    got = got.reshape(ranges, rows // ranges, head + 2)
    peaks = got[:, :, head]
    joint_peak = jnp.max(peaks, axis=0)
    factor = jnp.exp(peaks - joint_peak[None])
    joint_sum = jnp.sum(got[:, :, :head] * factor[:, :, None], axis=0)
    joint_total = jnp.sum(got[:, :, head + 1] * factor, axis=0)
    mine = (joint_sum / joint_total[:, None]).astype(jnp.bfloat16)

    spread = jnp.broadcast_to(mine[None], (ranges,) + mine.shape).reshape(rows, head)
    return lax.all_to_all(spread, "outer", 0, 0, tiled=True)


def solution(mesh):
    return jax.shard_map(
        on_device,
        mesh=mesh,
        in_specs=(P("inner", None), P(("outer", "inner"), None), P(("outer", "inner"), None)),
        out_specs=P("inner", None),
        check_vma=False,
    )
```

```python
import functools
import math

import jax
import jax.numpy as jnp
from jax import lax
from jax.experimental import pallas as pl
from jax.experimental.pallas import tpu as pltpu
from jax.sharding import PartitionSpec as P


def attend_kernel(scale, qt_ref, k_ref, vt_ref, acc_ref, m_ref, l_ref, acc, m_s, l_s):
    step = pl.program_id(1)

    @pl.when(step == 0)
    def _():
        acc[...] = jnp.zeros_like(acc)
        m_s[...] = jnp.full_like(m_s, -1e30)
        l_s[...] = jnp.zeros_like(l_s)

    scores = jnp.dot(k_ref[...], qt_ref[...], preferred_element_type=jnp.float32) * scale
    m_prev = m_s[...]
    m_new = jnp.maximum(m_prev, jnp.max(scores, axis=0, keepdims=True))
    rescale = jnp.exp(m_prev - m_new)
    probs = jnp.exp(scores - m_new)
    l_s[...] = l_s[...] * rescale + jnp.sum(probs, axis=0, keepdims=True)
    acc[...] = acc[...] * rescale + jnp.dot(
        vt_ref[...], probs.astype(jnp.bfloat16), preferred_element_type=jnp.float32
    )
    m_s[...] = m_new

    @pl.when(step == pl.num_programs(1) - 1)
    def _():
        acc_ref[...] = acc[...]
        m_ref[...] = m_s[...]
        l_ref[...] = l_s[...]


def local_partial(queries_t, keys, values_t, tq=1024, tk=512):
    tk = math.gcd(keys.shape[0], tk)
    head, rows = queries_t.shape
    count = keys.shape[0]
    scale = 1.0 / math.sqrt(head)
    grid = (rows // tq, count // tk)
    return pl.pallas_call(
        functools.partial(attend_kernel, scale),
        grid=grid,
        in_specs=[
            pl.BlockSpec((head, tq), lambda i, j: (0, i)),
            pl.BlockSpec((tk, head), lambda i, j: (j, 0)),
            pl.BlockSpec((head, tk), lambda i, j: (0, j)),
        ],
        out_specs=[
            pl.BlockSpec((head, tq), lambda i, j: (0, i)),
            pl.BlockSpec((1, tq), lambda i, j: (0, i)),
            pl.BlockSpec((1, tq), lambda i, j: (0, i)),
        ],
        out_shape=[
            jax.ShapeDtypeStruct((head, rows), jnp.float32),
            jax.ShapeDtypeStruct((1, rows), jnp.float32),
            jax.ShapeDtypeStruct((1, rows), jnp.float32),
        ],
        scratch_shapes=[
            pltpu.VMEM((head, tq), jnp.float32),
            pltpu.VMEM((1, tq), jnp.float32),
            pltpu.VMEM((1, tq), jnp.float32),
        ],
        compiler_params=pltpu.CompilerParams(dimension_semantics=("parallel", "arbitrary")),
        cost_estimate=pl.CostEstimate(
            flops=4 * rows * count * head,
            transcendentals=rows * count,
            bytes_accessed=rows * head * 6 + count * head * 4 * grid[0],
        ),
    )(queries_t, keys, values_t)


def split3(x):
    hi = x.astype(jnp.bfloat16)
    rest = x - hi.astype(jnp.float32)
    mid = rest.astype(jnp.bfloat16)
    lo = (rest - mid.astype(jnp.float32)).astype(jnp.bfloat16)
    return hi, mid, lo


def on_device(queries, key_rows, value_rows):
    rows, head = queries.shape
    kv = lax.all_gather(jnp.concatenate([key_rows, value_rows], axis=1), "inner", axis=0, tiled=True)
    acc_t, peak, total = local_partial(queries.T, kv[:, :head], kv[:, head:].T)

    ranges = lax.axis_size("outer")
    per = rows // ranges
    normed = (acc_t / total).T.astype(jnp.bfloat16).reshape(ranges, per, head)
    lse = (peak + jnp.log(total)).reshape(ranges, per)
    extra = jnp.concatenate(split3(lse) + (jnp.zeros((ranges, head - 3 * per), jnp.bfloat16),), axis=1)
    pad = jnp.zeros((ranges, 15, head), jnp.bfloat16)
    packed = jnp.concatenate([normed, extra[:, None, :], pad], axis=1)

    got = lax.all_to_all(packed, "outer", 0, 0)
    parts = got[:, per, :].astype(jnp.float32)
    lse_all = parts[:, :per] + parts[:, per:2 * per] + parts[:, 2 * per:3 * per]
    joint = jnp.max(lse_all, axis=0)
    weight = jnp.exp(lse_all - joint[None])
    summed = jnp.sum(got[:, :per, :].astype(jnp.float32) * weight[:, :, None], axis=0)
    mine = (summed / jnp.sum(weight, axis=0)[:, None]).astype(jnp.bfloat16)

    spread = jnp.broadcast_to(mine[None], (ranges,) + mine.shape)
    return lax.all_to_all(spread, "outer", 0, 0).reshape(rows, head)


def solution(mesh):
    return jax.shard_map(
        on_device,
        mesh=mesh,
        in_specs=(P("inner", None), P(("outer", "inner"), None), P(("outer", "inner"), None)),
        out_specs=P("inner", None),
        check_vma=False,
    )
```

```python
import functools
import math

import jax
import jax.numpy as jnp
from jax import lax
from jax.experimental import pallas as pl
from jax.experimental.pallas import tpu as pltpu
from jax.sharding import PartitionSpec as P


def attend_kernel(scale, q_ref, k_ref, v_ref, acc_ref, m_ref, l_ref, acc, m_s, l_s):
    step = pl.program_id(1)

    @pl.when(step == 0)
    def _():
        acc[...] = jnp.zeros_like(acc)
        m_s[...] = jnp.full_like(m_s, -1e30)
        l_s[...] = jnp.zeros_like(l_s)

    scores = (
        lax.dot_general(
            k_ref[...], q_ref[...], (((1,), (1,)), ((), ())), preferred_element_type=jnp.float32
        )
        * scale
    )
    m_prev = m_s[...]
    m_new = jnp.maximum(m_prev, jnp.max(scores, axis=0, keepdims=True))
    rescale = jnp.exp(m_prev - m_new)
    probs = jnp.exp(scores - m_new)
    l_s[...] = l_s[...] * rescale + jnp.sum(probs, axis=0, keepdims=True)
    acc[...] = acc[...] * rescale + lax.dot_general(
        v_ref[...], probs.astype(jnp.bfloat16), (((0,), (0,)), ((), ())),
        preferred_element_type=jnp.float32,
    )
    m_s[...] = m_new

    @pl.when(step == pl.num_programs(1) - 1)
    def _():
        acc_ref[...] = acc[...]
        m_ref[...] = m_s[...]
        l_ref[...] = l_s[...]


def local_partial(queries, kv, tq=1024, tk=512):
    tk = math.gcd(kv.shape[0], tk)
    rows, head = queries.shape
    count = kv.shape[0]
    scale = 1.0 / math.sqrt(head)
    grid = (rows // tq, count // tk)
    return pl.pallas_call(
        functools.partial(attend_kernel, scale),
        grid=grid,
        in_specs=[
            pl.BlockSpec((tq, head), lambda i, j: (i, 0)),
            pl.BlockSpec((tk, head), lambda i, j: (j, 0)),
            pl.BlockSpec((tk, head), lambda i, j: (j, 1)),
        ],
        out_specs=[
            pl.BlockSpec((head, tq), lambda i, j: (0, i)),
            pl.BlockSpec((1, tq), lambda i, j: (0, i)),
            pl.BlockSpec((1, tq), lambda i, j: (0, i)),
        ],
        out_shape=[
            jax.ShapeDtypeStruct((head, rows), jnp.float32),
            jax.ShapeDtypeStruct((1, rows), jnp.float32),
            jax.ShapeDtypeStruct((1, rows), jnp.float32),
        ],
        scratch_shapes=[
            pltpu.VMEM((head, tq), jnp.float32),
            pltpu.VMEM((1, tq), jnp.float32),
            pltpu.VMEM((1, tq), jnp.float32),
        ],
        compiler_params=pltpu.CompilerParams(dimension_semantics=("parallel", "arbitrary")),
        cost_estimate=pl.CostEstimate(
            flops=4 * rows * count * head,
            transcendentals=rows * count,
            bytes_accessed=rows * head * 6 + count * head * 4 * grid[0],
        ),
    )(queries, kv, kv)


def split3(x):
    hi = x.astype(jnp.bfloat16)
    rest = x - hi.astype(jnp.float32)
    mid = rest.astype(jnp.bfloat16)
    lo = (rest - mid.astype(jnp.float32)).astype(jnp.bfloat16)
    return hi, mid, lo


def on_device(queries, key_rows, value_rows):
    rows, head = queries.shape
    block = jnp.concatenate([key_rows, value_rows], axis=1)
    shards = lax.axis_size("inner")
    spread_kv = jnp.broadcast_to(block[None], (shards,) + block.shape)
    kv = lax.all_to_all(spread_kv, "inner", 0, 0).reshape(shards * block.shape[0], 2 * head)
    acc_t, peak, total = local_partial(queries, kv)

    ranges = lax.axis_size("outer")
    per = rows // ranges
    normed = (acc_t / total).T.astype(jnp.bfloat16).reshape(ranges, per, head)
    lse = (peak + jnp.log(total)).reshape(ranges, per)
    extra = jnp.concatenate(split3(lse) + (jnp.zeros((ranges, head - 3 * per), jnp.bfloat16),), axis=1)
    pad = jnp.zeros((ranges, 15, head), jnp.bfloat16)
    packed = jnp.concatenate([normed, extra[:, None, :], pad], axis=1)

    got = lax.all_to_all(packed, "outer", 0, 0)
    parts = got[:, per, :].astype(jnp.float32)
    lse_all = parts[:, :per] + parts[:, per:2 * per] + parts[:, 2 * per:3 * per]
    joint = jnp.max(lse_all, axis=0)
    weight = jnp.exp(lse_all - joint[None])
    summed = jnp.sum(got[:, :per, :].astype(jnp.float32) * weight[:, :, None], axis=0)
    mine = (summed / jnp.sum(weight, axis=0)[:, None]).astype(jnp.bfloat16)

    spread = jnp.broadcast_to(mine[None], (ranges,) + mine.shape)
    return lax.all_to_all(spread, "outer", 0, 0).reshape(rows, head)


def solution(mesh):
    return jax.shard_map(
        on_device,
        mesh=mesh,
        in_specs=(P("inner", None), P(("outer", "inner"), None), P(("outer", "inner"), None)),
        out_specs=P("inner", None),
        check_vma=False,
    )
```

```python
import functools
import math

import jax
import jax.numpy as jnp
from jax import lax
from jax.experimental import pallas as pl
from jax.experimental.pallas import tpu as pltpu
from jax.sharding import PartitionSpec as P


def attend_kernel(scale, q_ref, k_ref, v_ref, acc_ref, m_ref, l_ref, acc, m_s, l_s):
    step = pl.program_id(1)

    @pl.when(step == 0)
    def _():
        acc[...] = jnp.zeros_like(acc)
        m_s[...] = jnp.full_like(m_s, -1e30)
        l_s[...] = jnp.zeros_like(l_s)

    scores = (
        lax.dot_general(
            k_ref[...], q_ref[...], (((1,), (1,)), ((), ())), preferred_element_type=jnp.float32
        )
        * scale
    )
    m_prev = m_s[...]
    m_new = jnp.maximum(m_prev, jnp.max(scores, axis=0, keepdims=True))
    rescale = jnp.exp(m_prev - m_new)
    probs = jnp.exp(scores - m_new)
    l_s[...] = l_s[...] * rescale + jnp.sum(probs, axis=0, keepdims=True)
    acc[...] = acc[...] * rescale + lax.dot_general(
        v_ref[...], probs.astype(jnp.bfloat16), (((0,), (0,)), ((), ())),
        preferred_element_type=jnp.float32,
    )
    m_s[...] = m_new

    @pl.when(step == pl.num_programs(1) - 1)
    def _():
        acc_ref[...] = acc[...]
        m_ref[...] = m_s[...]
        l_ref[...] = l_s[...]


def local_partial(queries, kv, tq=1024, tk=2048):
    tk = math.gcd(kv.shape[0], tk)
    rows, head = queries.shape
    count = kv.shape[0]
    scale = 1.0 / math.sqrt(head)
    grid = (rows // tq, count // tk)
    return pl.pallas_call(
        functools.partial(attend_kernel, scale),
        grid=grid,
        in_specs=[
            pl.BlockSpec((tq, head), lambda i, j: (i, 0)),
            pl.BlockSpec((tk, head), lambda i, j: (j, 0)),
            pl.BlockSpec((tk, head), lambda i, j: (j, 1)),
        ],
        out_specs=[
            pl.BlockSpec((head, tq), lambda i, j: (0, i)),
            pl.BlockSpec((1, tq), lambda i, j: (0, i)),
            pl.BlockSpec((1, tq), lambda i, j: (0, i)),
        ],
        out_shape=[
            jax.ShapeDtypeStruct((head, rows), jnp.float32),
            jax.ShapeDtypeStruct((1, rows), jnp.float32),
            jax.ShapeDtypeStruct((1, rows), jnp.float32),
        ],
        scratch_shapes=[
            pltpu.VMEM((head, tq), jnp.float32),
            pltpu.VMEM((1, tq), jnp.float32),
            pltpu.VMEM((1, tq), jnp.float32),
        ],
        compiler_params=pltpu.CompilerParams(dimension_semantics=("parallel", "arbitrary")),
        cost_estimate=pl.CostEstimate(
            flops=4 * rows * count * head,
            transcendentals=rows * count,
            bytes_accessed=rows * head * 6 + count * head * 4 * grid[0],
        ),
    )(queries, kv, kv)


def split3(x):
    hi = x.astype(jnp.bfloat16)
    rest = x - hi.astype(jnp.float32)
    mid = rest.astype(jnp.bfloat16)
    lo = (rest - mid.astype(jnp.float32)).astype(jnp.bfloat16)
    return hi, mid, lo


def on_device(queries, key_rows, value_rows):
    rows, head = queries.shape
    block = jnp.concatenate([key_rows, value_rows], axis=1)
    shards = lax.axis_size("inner")
    spread_kv = jnp.broadcast_to(block[None], (shards,) + block.shape)
    kv = lax.all_to_all(spread_kv, "inner", 0, 0).reshape(shards * block.shape[0], 2 * head)
    acc_t, peak, total = local_partial(queries, kv)

    ranges = lax.axis_size("outer")
    per = rows // ranges
    normed = (acc_t / total).T.astype(jnp.bfloat16).reshape(ranges, per, head)
    lse = (peak + jnp.log(total)).reshape(ranges, per)
    extra = jnp.concatenate(split3(lse) + (jnp.zeros((ranges, head - 3 * per), jnp.bfloat16),), axis=1)
    pad = jnp.zeros((ranges, 7, head), jnp.bfloat16)
    packed = jnp.concatenate([normed, extra[:, None, :], pad], axis=1)

    got = lax.all_to_all(packed, "outer", 0, 0)
    parts = got[:, per, :].astype(jnp.float32)
    lse_all = parts[:, :per] + parts[:, per:2 * per] + parts[:, 2 * per:3 * per]
    joint = jnp.max(lse_all, axis=0)
    weight = jnp.exp(lse_all - joint[None])
    summed = jnp.sum(got[:, :per, :].astype(jnp.float32) * weight[:, :, None], axis=0)
    mine = (summed / jnp.sum(weight, axis=0)[:, None]).astype(jnp.bfloat16)

    spread = jnp.broadcast_to(mine[None], (ranges,) + mine.shape)
    return lax.all_to_all(spread, "outer", 0, 0).reshape(rows, head)


def solution(mesh):
    return jax.shard_map(
        on_device,
        mesh=mesh,
        in_specs=(P("inner", None), P(("outer", "inner"), None), P(("outer", "inner"), None)),
        out_specs=P("inner", None),
        check_vma=False,
    )
```

```python
import functools
import math

import jax
import jax.numpy as jnp
from jax import lax
from jax.experimental import pallas as pl
from jax.experimental.pallas import tpu as pltpu
from jax.sharding import PartitionSpec as P


def attend_kernel(scale, q_ref, k_ref, v_ref, acc_ref, m_ref, l_ref, acc, m_s, l_s):
    step = pl.program_id(1)

    @pl.when(step == 0)
    def _():
        acc[...] = jnp.zeros_like(acc)
        m_s[...] = jnp.full_like(m_s, -1e30)
        l_s[...] = jnp.zeros_like(l_s)

    scores = (
        lax.dot_general(
            k_ref[...], q_ref[...], (((1,), (1,)), ((), ())), preferred_element_type=jnp.float32
        )
        * scale
    )
    m_prev = m_s[...]
    m_new = jnp.maximum(m_prev, jnp.max(scores, axis=0, keepdims=True))
    rescale = jnp.exp(m_prev - m_new)
    probs = jnp.exp(scores - m_new)
    l_s[...] = l_s[...] * rescale + jnp.sum(probs, axis=0, keepdims=True)
    acc[...] = acc[...] * rescale + lax.dot_general(
        v_ref[...], probs.astype(jnp.bfloat16), (((0,), (0,)), ((), ())),
        preferred_element_type=jnp.float32,
    )
    m_s[...] = m_new

    @pl.when(step == pl.num_programs(1) - 1)
    def _():
        acc_ref[...] = acc[...]
        m_ref[...] = m_s[...]
        l_ref[...] = l_s[...]


def local_partial(queries, kv, tq=1024, tk=2048):
    tk = math.gcd(kv.shape[0], tk)
    rows, head = queries.shape
    count = kv.shape[0]
    scale = 1.0 / math.sqrt(head)
    grid = (rows // tq, count // tk)
    return pl.pallas_call(
        functools.partial(attend_kernel, scale),
        grid=grid,
        in_specs=[
            pl.BlockSpec((tq, head), lambda i, j: (i, 0)),
            pl.BlockSpec((tk, head), lambda i, j: (j, 0)),
            pl.BlockSpec((tk, head), lambda i, j: (j, 1)),
        ],
        out_specs=[
            pl.BlockSpec((head, tq), lambda i, j: (0, i)),
            pl.BlockSpec((1, tq), lambda i, j: (0, i)),
            pl.BlockSpec((1, tq), lambda i, j: (0, i)),
        ],
        out_shape=[
            jax.ShapeDtypeStruct((head, rows), jnp.float32),
            jax.ShapeDtypeStruct((1, rows), jnp.float32),
            jax.ShapeDtypeStruct((1, rows), jnp.float32),
        ],
        scratch_shapes=[
            pltpu.VMEM((head, tq), jnp.float32),
            pltpu.VMEM((1, tq), jnp.float32),
            pltpu.VMEM((1, tq), jnp.float32),
        ],
        compiler_params=pltpu.CompilerParams(dimension_semantics=("parallel", "arbitrary")),
        cost_estimate=pl.CostEstimate(
            flops=4 * rows * count * head,
            transcendentals=rows * count,
            bytes_accessed=rows * head * 6 + count * head * 4 * grid[0],
        ),
    )(queries, kv, kv)


def split3(x):
    hi = x.astype(jnp.bfloat16)
    rest = x - hi.astype(jnp.float32)
    mid = rest.astype(jnp.bfloat16)
    lo = (rest - mid.astype(jnp.float32)).astype(jnp.bfloat16)
    return hi, mid, lo


def on_device(queries, key_rows, value_rows):
    rows, head = queries.shape
    block = jnp.concatenate([key_rows, value_rows], axis=1)
    shards = lax.axis_size("inner")
    spread_kv = jnp.broadcast_to(block[None], (shards,) + block.shape)
    kv = lax.all_to_all(spread_kv, "inner", 0, 0).reshape(shards * block.shape[0], 2 * head)
    acc_t, peak, total = local_partial(queries, kv)

    ranges = lax.axis_size("outer")
    per = rows // ranges
    normed = (acc_t / total).T.astype(jnp.bfloat16).reshape(ranges, per, head)
    lse = (peak + jnp.log(total)).reshape(ranges, per)
    extra = jnp.concatenate(split3(lse) + (jnp.zeros((ranges, head - 3 * per), jnp.bfloat16),), axis=1)
    pad = jnp.zeros((ranges, 7, head), jnp.bfloat16)
    packed = jnp.concatenate([normed, extra[:, None, :], pad], axis=1)

    me = lax.axis_index("outer")
    offsets = jnp.arange(ranges)
    outbox = jnp.take(packed, (me + offsets) % ranges, axis=0)
    inbox = [outbox[0]] + [
        lax.ppermute(outbox[d], "outer", [(j, (j + d) % ranges) for j in range(ranges)])
        for d in range(1, ranges)
    ]
    got = jnp.stack(inbox)
    parts = got[:, per, :].astype(jnp.float32)
    lse_all = parts[:, :per] + parts[:, per:2 * per] + parts[:, 2 * per:3 * per]
    joint = jnp.max(lse_all, axis=0)
    weight = jnp.exp(lse_all - joint[None])
    summed = jnp.sum(got[:, :per, :].astype(jnp.float32) * weight[:, :, None], axis=0)
    mine = (summed / jnp.sum(weight, axis=0)[:, None]).astype(jnp.bfloat16)

    arrived = jnp.stack([mine] + [
        lax.ppermute(mine, "outer", [(j, (j + d) % ranges) for j in range(ranges)])
        for d in range(1, ranges)
    ])
    return jnp.take(arrived, (me - offsets) % ranges, axis=0).reshape(rows, head)


def solution(mesh):
    return jax.shard_map(
        on_device,
        mesh=mesh,
        in_specs=(P("inner", None), P(("outer", "inner"), None), P(("outer", "inner"), None)),
        out_specs=P("inner", None),
        check_vma=False,
    )
```

```python
import functools
import math

import jax
import jax.numpy as jnp
from jax import lax
from jax.experimental import pallas as pl
from jax.experimental.pallas import tpu as pltpu
from jax.sharding import PartitionSpec as P


def attend_kernel(scale, tk, q_ref, kv_ref, normed_ref, lse_ref):
    head = q_ref.shape[1]
    queries = q_ref[...]
    peak = total = acc = None
    for start in range(0, kv_ref.shape[0], tk):
        keys = kv_ref[start:start + tk, :head]
        values = kv_ref[start:start + tk, head:]
        scores = (
            lax.dot_general(
                keys, queries, (((1,), (1,)), ((), ())), preferred_element_type=jnp.float32
            )
            * scale
        )
        tile_peak = jnp.max(scores, axis=0, keepdims=True)
        new_peak = tile_peak if peak is None else jnp.maximum(peak, tile_peak)
        probs = jnp.exp(scores - new_peak)
        tile_total = jnp.sum(probs, axis=0, keepdims=True)
        tile_acc = lax.dot_general(
            values, probs.astype(jnp.bfloat16), (((0,), (0,)), ((), ())),
            preferred_element_type=jnp.float32,
        )
        if peak is None:
            total, acc = tile_total, tile_acc
        else:
            rescale = jnp.exp(peak - new_peak)
            total = total * rescale + tile_total
            acc = acc * rescale + tile_acc
        peak = new_peak
    normed_ref[...] = (acc / total).T.astype(normed_ref.dtype)
    lse_ref[...] = peak + jnp.log(total)


def local_partial(queries, kv, tk=2048):
    tk = math.gcd(kv.shape[0], tk)
    rows, head = queries.shape
    count = kv.shape[0]
    scale = 1.0 / math.sqrt(head)
    whole = pl.BlockSpec(memory_space=pltpu.VMEM)
    return pl.pallas_call(
        functools.partial(attend_kernel, scale, tk),
        in_specs=[whole, whole],
        out_specs=[whole, whole],
        out_shape=[
            jax.ShapeDtypeStruct((rows, head), jnp.bfloat16),
            jax.ShapeDtypeStruct((1, rows), jnp.float32),
        ],
        cost_estimate=pl.CostEstimate(
            flops=4 * rows * count * head,
            transcendentals=rows * count,
            bytes_accessed=rows * head * 4 + count * head * 4,
        ),
    )(queries, kv)


def split3(x):
    hi = x.astype(jnp.bfloat16)
    rest = x - hi.astype(jnp.float32)
    mid = rest.astype(jnp.bfloat16)
    lo = (rest - mid.astype(jnp.float32)).astype(jnp.bfloat16)
    return hi, mid, lo


def on_device(queries, key_rows, value_rows):
    rows, head = queries.shape
    shards = lax.axis_size("inner")
    spread_kv = jnp.concatenate(
        [jnp.broadcast_to(part[None], (shards,) + part.shape) for part in (key_rows, value_rows)], axis=2
    )
    kv = lax.all_to_all(spread_kv, "inner", 0, 0).reshape(shards * key_rows.shape[0], 2 * head)
    normed, lse = local_partial(queries, kv)

    ranges = lax.axis_size("outer")
    per = rows // ranges
    normed = normed.reshape(ranges, per, head)
    lse = lse.reshape(ranges, per)
    extra = jnp.concatenate(split3(lse) + (jnp.zeros((ranges, head - 3 * per), jnp.bfloat16),), axis=1)
    pad = jnp.zeros((ranges, 7, head), jnp.bfloat16)
    packed = jnp.concatenate([normed, extra[:, None, :], pad], axis=1)

    got = lax.all_to_all(packed, "outer", 0, 0)
    parts = got[:, per, :].astype(jnp.float32)
    lse_all = parts[:, :per] + parts[:, per:2 * per] + parts[:, 2 * per:3 * per]
    joint = jnp.max(lse_all, axis=0)
    weight = jnp.exp(lse_all - joint[None])
    summed = jnp.sum(got[:, :per, :].astype(jnp.float32) * weight[:, :, None], axis=0)
    mine = (summed / jnp.sum(weight, axis=0)[:, None]).astype(jnp.bfloat16)

    spread = jnp.broadcast_to(mine[None], (ranges,) + mine.shape)
    return lax.all_to_all(spread, "outer", 0, 0).reshape(rows, head)


def solution(mesh):
    return jax.shard_map(
        on_device,
        mesh=mesh,
        in_specs=(P("inner", None), P(("outer", "inner"), None), P(("outer", "inner"), None)),
        out_specs=P("inner", None),
        check_vma=False,
    )
```

```python
import functools
import math

import jax
import jax.numpy as jnp
from jax import lax
from jax.experimental import pallas as pl
from jax.experimental.pallas import tpu as pltpu
from jax.sharding import PartitionSpec as P


def attend_kernel(scale, q_ref, k_ref, v_ref, acc_ref, m_ref, l_ref, acc, m_s, l_s):
    step = pl.program_id(1)

    @pl.when(step == 0)
    def _():
        acc[...] = jnp.zeros_like(acc)
        m_s[...] = jnp.full_like(m_s, -1e30)
        l_s[...] = jnp.zeros_like(l_s)

    scores = (
        lax.dot_general(
            k_ref[...], q_ref[...], (((1,), (1,)), ((), ())), preferred_element_type=jnp.float32
        )
        * scale
    )
    m_prev = m_s[...]
    m_new = jnp.maximum(m_prev, jnp.max(scores, axis=0, keepdims=True))
    rescale = jnp.exp(m_prev - m_new)
    probs = jnp.exp(scores - m_new)
    values = jnp.concatenate([v_ref[...], jnp.ones_like(v_ref[...])], axis=1)
    both = lax.dot_general(
        values, probs.astype(jnp.bfloat16), (((0,), (0,)), ((), ())),
        preferred_element_type=jnp.float32,
    )
    head = v_ref.shape[1]
    l_s[...] = l_s[...] * rescale + both[head:head + 1]
    acc[...] = acc[...] * rescale + both[:head]
    m_s[...] = m_new

    @pl.when(step == pl.num_programs(1) - 1)
    def _():
        acc_ref[...] = acc[...]
        m_ref[...] = m_s[...]
        l_ref[...] = l_s[...]


def local_partial(queries, kv, tq=1024, tk=2048):
    tk = math.gcd(kv.shape[0], tk)
    rows, head = queries.shape
    count = kv.shape[0]
    scale = 1.0 / math.sqrt(head)
    grid = (rows // tq, count // tk)
    return pl.pallas_call(
        functools.partial(attend_kernel, scale),
        grid=grid,
        in_specs=[
            pl.BlockSpec((tq, head), lambda i, j: (i, 0)),
            pl.BlockSpec((tk, head), lambda i, j: (j, 0)),
            pl.BlockSpec((tk, head), lambda i, j: (j, 1)),
        ],
        out_specs=[
            pl.BlockSpec((head, tq), lambda i, j: (0, i)),
            pl.BlockSpec((1, tq), lambda i, j: (0, i)),
            pl.BlockSpec((1, tq), lambda i, j: (0, i)),
        ],
        out_shape=[
            jax.ShapeDtypeStruct((head, rows), jnp.float32),
            jax.ShapeDtypeStruct((1, rows), jnp.float32),
            jax.ShapeDtypeStruct((1, rows), jnp.float32),
        ],
        scratch_shapes=[
            pltpu.VMEM((head, tq), jnp.float32),
            pltpu.VMEM((1, tq), jnp.float32),
            pltpu.VMEM((1, tq), jnp.float32),
        ],
        compiler_params=pltpu.CompilerParams(dimension_semantics=("parallel", "arbitrary")),
        cost_estimate=pl.CostEstimate(
            flops=4 * rows * count * head,
            transcendentals=rows * count,
            bytes_accessed=rows * head * 6 + count * head * 4 * grid[0],
        ),
    )(queries, kv, kv)


def split3(x):
    hi = x.astype(jnp.bfloat16)
    rest = x - hi.astype(jnp.float32)
    mid = rest.astype(jnp.bfloat16)
    lo = (rest - mid.astype(jnp.float32)).astype(jnp.bfloat16)
    return hi, mid, lo


def on_device(queries, key_rows, value_rows):
    rows, head = queries.shape
    block = jnp.concatenate([key_rows, value_rows], axis=1)
    shards = lax.axis_size("inner")
    spread_kv = jnp.broadcast_to(block[None], (shards,) + block.shape)
    kv = lax.all_to_all(spread_kv, "inner", 0, 0).reshape(shards * block.shape[0], 2 * head)
    acc_t, peak, total = local_partial(queries, kv)

    ranges = lax.axis_size("outer")
    per = rows // ranges
    normed = (acc_t / total).T.astype(jnp.bfloat16).reshape(ranges, per, head)
    lse = (peak + jnp.log(total)).reshape(ranges, per)
    extra = jnp.concatenate(split3(lse) + (jnp.zeros((ranges, head - 3 * per), jnp.bfloat16),), axis=1)
    pad = jnp.zeros((ranges, 7, head), jnp.bfloat16)
    packed = jnp.concatenate([normed, extra[:, None, :], pad], axis=1)

    got = lax.all_to_all(packed, "outer", 0, 0)
    parts = got[:, per, :].astype(jnp.float32)
    lse_all = parts[:, :per] + parts[:, per:2 * per] + parts[:, 2 * per:3 * per]
    joint = jnp.max(lse_all, axis=0)
    weight = jnp.exp(lse_all - joint[None])
    summed = jnp.sum(got[:, :per, :].astype(jnp.float32) * weight[:, :, None], axis=0)
    mine = (summed / jnp.sum(weight, axis=0)[:, None]).astype(jnp.bfloat16)

    spread = jnp.broadcast_to(mine[None], (ranges,) + mine.shape)
    return lax.all_to_all(spread, "outer", 0, 0).reshape(rows, head)


def solution(mesh):
    return jax.shard_map(
        on_device,
        mesh=mesh,
        in_specs=(P("inner", None), P(("outer", "inner"), None), P(("outer", "inner"), None)),
        out_specs=P("inner", None),
        check_vma=False,
    )
```

```python
import functools
import math

import jax
import jax.numpy as jnp
from jax import lax
from jax.experimental import pallas as pl
from jax.experimental.pallas import tpu as pltpu
from jax.sharding import PartitionSpec as P


def attend_kernel(scale, q_ref, k_ref, v_ref, acc_ref, m_ref, l_ref, acc, m_s, l_s):
    step = pl.program_id(1)

    @pl.when(step == 0)
    def _():
        acc[...] = jnp.zeros_like(acc)
        m_s[...] = jnp.full_like(m_s, -1e30)
        l_s[...] = jnp.zeros_like(l_s)

    scores = (
        lax.dot_general(
            k_ref[...], q_ref[...], (((1,), (1,)), ((), ())), preferred_element_type=jnp.float32
        )
        * scale
    )
    m_prev = m_s[...]
    m_new = jnp.maximum(m_prev, jnp.max(scores, axis=0, keepdims=True))
    rescale = jnp.exp(m_prev - m_new)
    probs = jnp.exp(scores - m_new)
    values = jnp.concatenate([v_ref[...], jnp.ones_like(v_ref[...])], axis=1)
    both = lax.dot_general(
        values, probs.astype(jnp.bfloat16), (((0,), (0,)), ((), ())),
        preferred_element_type=jnp.float32,
    )
    head = v_ref.shape[1]
    l_s[...] = l_s[...] * rescale + both[head:head + 1]
    acc[...] = acc[...] * rescale + both[:head]
    m_s[...] = m_new

    @pl.when(step == pl.num_programs(1) - 1)
    def _():
        acc_ref[...] = acc[...]
        m_ref[...] = m_s[...]
        l_ref[...] = l_s[...]


def local_partial(queries, kv, tq=1024, tk=2048):
    tk = math.gcd(kv.shape[0], tk)
    rows, head = queries.shape
    count = kv.shape[0]
    scale = 1.0 / math.sqrt(head)
    grid = (rows // tq, count // tk)
    return pl.pallas_call(
        functools.partial(attend_kernel, scale),
        grid=grid,
        in_specs=[
            pl.BlockSpec((tq, head), lambda i, j: (i, 0)),
            pl.BlockSpec((tk, head), lambda i, j: (j, 0)),
            pl.BlockSpec((tk, head), lambda i, j: (j, 1)),
        ],
        out_specs=[
            pl.BlockSpec((head, tq), lambda i, j: (0, i)),
            pl.BlockSpec((1, tq), lambda i, j: (0, i)),
            pl.BlockSpec((1, tq), lambda i, j: (0, i)),
        ],
        out_shape=[
            jax.ShapeDtypeStruct((head, rows), jnp.float32),
            jax.ShapeDtypeStruct((1, rows), jnp.float32),
            jax.ShapeDtypeStruct((1, rows), jnp.float32),
        ],
        scratch_shapes=[
            pltpu.VMEM((head, tq), jnp.float32),
            pltpu.VMEM((1, tq), jnp.float32),
            pltpu.VMEM((1, tq), jnp.float32),
        ],
        compiler_params=pltpu.CompilerParams(dimension_semantics=("parallel", "arbitrary")),
        cost_estimate=pl.CostEstimate(
            flops=4 * rows * count * head,
            transcendentals=rows * count,
            bytes_accessed=rows * head * 6 + count * head * 4 * grid[0],
        ),
    )(queries, kv, kv)


def split3(x):
    hi = x.astype(jnp.bfloat16)
    rest = x - hi.astype(jnp.float32)
    mid = rest.astype(jnp.bfloat16)
    lo = (rest - mid.astype(jnp.float32)).astype(jnp.bfloat16)
    return hi, mid, lo


def on_device(queries, key_rows, value_rows):
    rows, head = queries.shape
    block = jnp.concatenate([key_rows, value_rows], axis=1)
    shards = lax.axis_size("inner")
    same_core = [list(range(core, shards, 2)) for core in range(2)]
    chip = [[j, j + 1] for j in range(0, shards, 2)]
    spread_kv = jnp.broadcast_to(block[None], (shards // 2,) + block.shape)
    half = lax.all_to_all(spread_kv, "inner", 0, 0, axis_index_groups=same_core)
    half = half.reshape(shards // 2 * block.shape[0], 2 * head)
    both = lax.all_to_all(jnp.broadcast_to(half[None], (2,) + half.shape), "inner", 0, 0, axis_index_groups=chip)
    kv = both.reshape(shards * block.shape[0], 2 * head)
    acc_t, peak, total = local_partial(queries, kv)

    ranges = lax.axis_size("outer")
    per = rows // ranges
    normed = (acc_t / total).T.astype(jnp.bfloat16).reshape(ranges, per, head)
    lse = (peak + jnp.log(total)).reshape(ranges, per)
    extra = jnp.concatenate(split3(lse) + (jnp.zeros((ranges, head - 3 * per), jnp.bfloat16),), axis=1)
    pad = jnp.zeros((ranges, 7, head), jnp.bfloat16)
    packed = jnp.concatenate([normed, extra[:, None, :], pad], axis=1)

    got = lax.all_to_all(packed, "outer", 0, 0)
    parts = got[:, per, :].astype(jnp.float32)
    lse_all = parts[:, :per] + parts[:, per:2 * per] + parts[:, 2 * per:3 * per]
    joint = jnp.max(lse_all, axis=0)
    weight = jnp.exp(lse_all - joint[None])
    summed = jnp.sum(got[:, :per, :].astype(jnp.float32) * weight[:, :, None], axis=0)
    mine = (summed / jnp.sum(weight, axis=0)[:, None]).astype(jnp.bfloat16)

    spread = jnp.broadcast_to(mine[None], (ranges,) + mine.shape)
    return lax.all_to_all(spread, "outer", 0, 0).reshape(rows, head)


def solution(mesh):
    return jax.shard_map(
        on_device,
        mesh=mesh,
        in_specs=(P("inner", None), P(("outer", "inner"), None), P(("outer", "inner"), None)),
        out_specs=P("inner", None),
        check_vma=False,
    )
```

```python
import functools
import math

import jax
import jax.numpy as jnp
from jax import lax
from jax.experimental import pallas as pl
from jax.experimental.pallas import tpu as pltpu
from jax.sharding import PartitionSpec as P


def attend_kernel(scale, q_ref, k_ref, v_ref, acc0, m0, l0, acc_ref, m_ref, l_ref, acc, m_s, l_s):
    step = pl.program_id(1)

    @pl.when(step == 0)
    def _():
        acc[...] = acc0[...]
        m_s[...] = m0[...]
        l_s[...] = l0[...]

    scores = (
        lax.dot_general(
            k_ref[...], q_ref[...], (((1,), (1,)), ((), ())), preferred_element_type=jnp.float32
        )
        * scale
    )
    m_prev = m_s[...]
    m_new = jnp.maximum(m_prev, jnp.max(scores, axis=0, keepdims=True))
    rescale = jnp.exp(m_prev - m_new)
    probs = jnp.exp(scores - m_new)
    values = jnp.concatenate([v_ref[...], jnp.ones_like(v_ref[...])], axis=1)
    both = lax.dot_general(
        values, probs.astype(jnp.bfloat16), (((0,), (0,)), ((), ())),
        preferred_element_type=jnp.float32,
    )
    head = v_ref.shape[1]
    l_s[...] = l_s[...] * rescale + both[head:head + 1]
    acc[...] = acc[...] * rescale + both[:head]
    m_s[...] = m_new

    @pl.when(step == pl.num_programs(1) - 1)
    def _():
        acc_ref[...] = acc[...]
        m_ref[...] = m_s[...]
        l_ref[...] = l_s[...]


def local_partial(queries, kv, state=None, tq=1024, tk=2048):
    tk = math.gcd(kv.shape[0], tk)
    rows, head = queries.shape
    count = kv.shape[0]
    scale = 1.0 / math.sqrt(head)
    grid = (rows // tq, count // tk)
    if state is None:
        state = (
            jnp.zeros((head, rows), jnp.float32),
            jnp.full((1, rows), -1e30, jnp.float32),
            jnp.zeros((1, rows), jnp.float32),
        )
    return pl.pallas_call(
        functools.partial(attend_kernel, scale),
        grid=grid,
        in_specs=[
            pl.BlockSpec((tq, head), lambda i, j: (i, 0)),
            pl.BlockSpec((tk, head), lambda i, j: (j, 0)),
            pl.BlockSpec((tk, head), lambda i, j: (j, 1)),
            pl.BlockSpec((head, tq), lambda i, j: (0, i)),
            pl.BlockSpec((1, tq), lambda i, j: (0, i)),
            pl.BlockSpec((1, tq), lambda i, j: (0, i)),
        ],
        out_specs=[
            pl.BlockSpec((head, tq), lambda i, j: (0, i)),
            pl.BlockSpec((1, tq), lambda i, j: (0, i)),
            pl.BlockSpec((1, tq), lambda i, j: (0, i)),
        ],
        out_shape=[
            jax.ShapeDtypeStruct((head, rows), jnp.float32),
            jax.ShapeDtypeStruct((1, rows), jnp.float32),
            jax.ShapeDtypeStruct((1, rows), jnp.float32),
        ],
        scratch_shapes=[
            pltpu.VMEM((head, tq), jnp.float32),
            pltpu.VMEM((1, tq), jnp.float32),
            pltpu.VMEM((1, tq), jnp.float32),
        ],
        compiler_params=pltpu.CompilerParams(dimension_semantics=("parallel", "arbitrary")),
        cost_estimate=pl.CostEstimate(
            flops=4 * rows * count * head,
            transcendentals=rows * count,
            bytes_accessed=rows * head * 10 + count * head * 4 * grid[0],
        ),
    )(queries, kv, kv, *state)


def split3(x):
    hi = x.astype(jnp.bfloat16)
    rest = x - hi.astype(jnp.float32)
    mid = rest.astype(jnp.bfloat16)
    lo = (rest - mid.astype(jnp.float32)).astype(jnp.bfloat16)
    return hi, mid, lo


def on_device(queries, key_rows, value_rows):
    rows, head = queries.shape
    block = jnp.concatenate([key_rows, value_rows], axis=1)
    shards = lax.axis_size("inner")
    same_core = [list(range(core, shards, 2)) for core in range(2)]
    chip = [[j, j + 1] for j in range(0, shards, 2)]
    spread_kv = jnp.broadcast_to(block[None], (shards // 2,) + block.shape)
    half = lax.all_to_all(spread_kv, "inner", 0, 0, axis_index_groups=same_core)
    half = half.reshape(shards // 2 * block.shape[0], 2 * head)
    state = local_partial(queries, half)
    both = lax.all_to_all(jnp.broadcast_to(half[None], (2,) + half.shape), "inner", 0, 0, axis_index_groups=chip)
    other = lax.dynamic_index_in_dim(both, 1 - lax.axis_index("inner") % 2, 0, keepdims=False)
    acc_t, peak, total = local_partial(queries, other, state)

    ranges = lax.axis_size("outer")
    per = rows // ranges
    normed = (acc_t / total).T.astype(jnp.bfloat16).reshape(ranges, per, head)
    lse = (peak + jnp.log(total)).reshape(ranges, per)
    extra = jnp.concatenate(split3(lse) + (jnp.zeros((ranges, head - 3 * per), jnp.bfloat16),), axis=1)
    pad = jnp.zeros((ranges, 7, head), jnp.bfloat16)
    packed = jnp.concatenate([normed, extra[:, None, :], pad], axis=1)

    got = lax.all_to_all(packed, "outer", 0, 0)
    parts = got[:, per, :].astype(jnp.float32)
    lse_all = parts[:, :per] + parts[:, per:2 * per] + parts[:, 2 * per:3 * per]
    joint = jnp.max(lse_all, axis=0)
    weight = jnp.exp(lse_all - joint[None])
    summed = jnp.sum(got[:, :per, :].astype(jnp.float32) * weight[:, :, None], axis=0)
    mine = (summed / jnp.sum(weight, axis=0)[:, None]).astype(jnp.bfloat16)

    spread = jnp.broadcast_to(mine[None], (ranges,) + mine.shape)
    return lax.all_to_all(spread, "outer", 0, 0).reshape(rows, head)


def solution(mesh):
    return jax.shard_map(
        on_device,
        mesh=mesh,
        in_specs=(P("inner", None), P(("outer", "inner"), None), P(("outer", "inner"), None)),
        out_specs=P("inner", None),
        check_vma=False,
    )
```

```python
import functools
import math

import jax
import jax.numpy as jnp
from jax import lax
from jax.experimental import pallas as pl
from jax.experimental.pallas import tpu as pltpu
from jax.sharding import PartitionSpec as P


def attend_kernel(scale, q_ref, k_ref, v_ref, acc_ref, m_ref, l_ref, acc, m_s, l_s):
    step = pl.program_id(1)

    @pl.when(step == 0)
    def _():
        acc[...] = jnp.zeros_like(acc)
        m_s[...] = jnp.full_like(m_s, -1e30)
        l_s[...] = jnp.zeros_like(l_s)

    scores = (
        lax.dot_general(
            k_ref[...], q_ref[...], (((1,), (1,)), ((), ())), preferred_element_type=jnp.float32
        )
        * scale
    )
    m_prev = m_s[...]
    m_new = jnp.maximum(m_prev, jnp.max(scores, axis=0, keepdims=True))
    rescale = jnp.exp(m_prev - m_new)
    probs = jnp.exp(scores - m_new)
    values = jnp.concatenate([v_ref[...], jnp.ones_like(v_ref[...])], axis=1)
    both = lax.dot_general(
        values, probs.astype(jnp.bfloat16), (((0,), (0,)), ((), ())),
        preferred_element_type=jnp.float32,
    )
    head = v_ref.shape[1]
    l_s[...] = l_s[...] * rescale + both[head:head + 1]
    acc[...] = acc[...] * rescale + both[:head]
    m_s[...] = m_new

    @pl.when(step == pl.num_programs(1) - 1)
    def _():
        acc_ref[...] = acc[...]
        m_ref[...] = m_s[...]
        l_ref[...] = l_s[...]


def local_partial(queries, kv, tq=1024, tk=2048):
    tk = math.gcd(kv.shape[0], tk)
    rows, head = queries.shape
    count = kv.shape[0]
    scale = 1.0 / math.sqrt(head)
    grid = (rows // tq, count // tk)
    return pl.pallas_call(
        functools.partial(attend_kernel, scale),
        grid=grid,
        in_specs=[
            pl.BlockSpec((tq, head), lambda i, j: (i, 0)),
            pl.BlockSpec((tk, head), lambda i, j: (j, 0)),
            pl.BlockSpec((tk, head), lambda i, j: (j, 1)),
        ],
        out_specs=[
            pl.BlockSpec((head, tq), lambda i, j: (0, i)),
            pl.BlockSpec((1, tq), lambda i, j: (0, i)),
            pl.BlockSpec((1, tq), lambda i, j: (0, i)),
        ],
        out_shape=[
            jax.ShapeDtypeStruct((head, rows), jnp.float32),
            jax.ShapeDtypeStruct((1, rows), jnp.float32),
            jax.ShapeDtypeStruct((1, rows), jnp.float32),
        ],
        scratch_shapes=[
            pltpu.VMEM((head, tq), jnp.float32),
            pltpu.VMEM((1, tq), jnp.float32),
            pltpu.VMEM((1, tq), jnp.float32),
        ],
        compiler_params=pltpu.CompilerParams(dimension_semantics=("parallel", "arbitrary")),
        cost_estimate=pl.CostEstimate(
            flops=4 * rows * count * head,
            transcendentals=rows * count,
            bytes_accessed=rows * head * 6 + count * head * 4 * grid[0],
        ),
    )(queries, kv, kv)


def split3(x):
    hi = x.astype(jnp.bfloat16)
    rest = x - hi.astype(jnp.float32)
    mid = rest.astype(jnp.bfloat16)
    lo = (rest - mid.astype(jnp.float32)).astype(jnp.bfloat16)
    return hi, mid, lo


def on_device(queries, key_rows, value_rows):
    rows, head = queries.shape
    block = jnp.concatenate([key_rows, value_rows], axis=1)
    shards = lax.axis_size("inner")
    same_core = [list(range(core, shards, 2)) for core in range(2)]
    chip = [[j, j + 1] for j in range(0, shards, 2)]
    spread_kv = jnp.broadcast_to(block[None], (shards // 2,) + block.shape)
    half = lax.all_to_all(spread_kv, "inner", 0, 0, axis_index_groups=same_core)
    half = half.reshape(shards // 2 * block.shape[0], 2 * head)
    both = lax.all_to_all(jnp.broadcast_to(half[None], (2,) + half.shape), "inner", 0, 0, axis_index_groups=chip)
    kv = both.reshape(shards * block.shape[0], 2 * head)
    acc_t, peak, total = local_partial(queries, kv)

    normed = (acc_t / total).T
    lse = (peak + jnp.log(total)).reshape(rows)

    ranges = lax.axis_size("outer")
    me = lax.axis_index("outer")
    partners = [[j, j + 1] for j in range(0, ranges, 2)]
    along_z = [list(range(side, ranges, 2)) for side in range(2)]
    normed, lse = merge_step(normed, lse, 2, partners)
    normed, lse = merge_step(normed, lse, ranges // 2, along_z)
    mine = normed.astype(jnp.bfloat16)

    spread = jnp.broadcast_to(mine[None], (ranges // 2,) + mine.shape)
    half = lax.all_to_all(spread, "outer", 0, 0, axis_index_groups=along_z).reshape(-1, head)
    spread = jnp.broadcast_to(half[None], (2,) + half.shape)
    return lax.all_to_all(spread, "outer", 0, 0, axis_index_groups=partners).reshape(rows, head)


def merge_step(normed, lse, members, groups):
    rows, head = normed.shape
    per = rows // members
    tile = -(-3 * per // head)
    tile = -(-tile // 8) * 8
    payload = normed.astype(jnp.bfloat16).reshape(members, per, head)
    parts = jnp.concatenate(split3(lse.reshape(members, per)), axis=1)
    parts = jnp.pad(parts, ((0, 0), (0, tile * head - 3 * per))).reshape(members, tile, head)
    got = lax.all_to_all(jnp.concatenate([payload, parts], axis=1), "outer", 0, 0, axis_index_groups=groups)
    pieces = got[:, per:, :].reshape(members, tile * head)[:, :3 * per].astype(jnp.float32)
    lse_all = pieces[:, :per] + pieces[:, per:2 * per] + pieces[:, 2 * per:]
    joint = jnp.max(lse_all, axis=0)
    weight = jnp.exp(lse_all - joint[None])
    weight_sum = jnp.sum(weight, axis=0)
    summed = jnp.sum(got[:, :per, :].astype(jnp.float32) * weight[:, :, None], axis=0)
    return summed / weight_sum[:, None], joint + jnp.log(weight_sum)


def solution(mesh):
    return jax.shard_map(
        on_device,
        mesh=mesh,
        in_specs=(P("inner", None), P(("outer", "inner"), None), P(("outer", "inner"), None)),
        out_specs=P("inner", None),
        check_vma=False,
    )
```

```python
import functools
import math

import jax
import jax.numpy as jnp
from jax import lax
from jax.experimental import pallas as pl
from jax.experimental.pallas import tpu as pltpu
from jax.sharding import PartitionSpec as P


def attend_kernel(scale, q_ref, k_ref, v_ref, acc_ref, m_ref, l_ref, acc, m_s, l_s):
    step = pl.program_id(1)

    @pl.when(step == 0)
    def _():
        acc[...] = jnp.zeros_like(acc)
        m_s[...] = jnp.full_like(m_s, -1e30)
        l_s[...] = jnp.zeros_like(l_s)

    scores = (
        lax.dot_general(
            k_ref[...], q_ref[...], (((1,), (1,)), ((), ())), preferred_element_type=jnp.float32
        )
        * scale
    )
    m_prev = m_s[...]
    m_new = jnp.maximum(m_prev, jnp.max(scores, axis=0, keepdims=True))
    rescale = jnp.exp(m_prev - m_new)
    probs = jnp.exp(scores - m_new)
    values = jnp.concatenate([v_ref[...], jnp.ones_like(v_ref[...])], axis=1)
    both = lax.dot_general(
        values, probs.astype(jnp.bfloat16), (((0,), (0,)), ((), ())),
        preferred_element_type=jnp.float32,
    )
    head = v_ref.shape[1]
    l_s[...] = l_s[...] * rescale + both[head:head + 1]
    acc[...] = acc[...] * rescale + both[:head]
    m_s[...] = m_new

    @pl.when(step == pl.num_programs(1) - 1)
    def _():
        acc_ref[...] = acc[...]
        m_ref[...] = m_s[...]
        l_ref[...] = l_s[...]


def local_partial(queries, kv, tq=1024, tk=2048):
    tk = math.gcd(kv.shape[0], tk)
    rows, head = queries.shape
    count = kv.shape[0]
    scale = 1.0 / math.sqrt(head)
    grid = (rows // tq, count // tk)
    return pl.pallas_call(
        functools.partial(attend_kernel, scale),
        grid=grid,
        in_specs=[
            pl.BlockSpec((tq, head), lambda i, j: (i, 0)),
            pl.BlockSpec((tk, head), lambda i, j: (j, 0)),
            pl.BlockSpec((tk, head), lambda i, j: (j, 1)),
        ],
        out_specs=[
            pl.BlockSpec((head, tq), lambda i, j: (0, i)),
            pl.BlockSpec((1, tq), lambda i, j: (0, i)),
            pl.BlockSpec((1, tq), lambda i, j: (0, i)),
        ],
        out_shape=[
            jax.ShapeDtypeStruct((head, rows), jnp.float32),
            jax.ShapeDtypeStruct((1, rows), jnp.float32),
            jax.ShapeDtypeStruct((1, rows), jnp.float32),
        ],
        scratch_shapes=[
            pltpu.VMEM((head, tq), jnp.float32),
            pltpu.VMEM((1, tq), jnp.float32),
            pltpu.VMEM((1, tq), jnp.float32),
        ],
        compiler_params=pltpu.CompilerParams(dimension_semantics=("parallel", "arbitrary")),
        cost_estimate=pl.CostEstimate(
            flops=4 * rows * count * head,
            transcendentals=rows * count,
            bytes_accessed=rows * head * 6 + count * head * 4 * grid[0],
        ),
    )(queries, kv, kv)


def split3(x):
    hi = x.astype(jnp.bfloat16)
    rest = x - hi.astype(jnp.float32)
    mid = rest.astype(jnp.bfloat16)
    lo = (rest - mid.astype(jnp.float32)).astype(jnp.bfloat16)
    return hi, mid, lo


def on_device(queries, key_rows, value_rows):
    rows, head = queries.shape
    block = jnp.concatenate([key_rows, value_rows], axis=1)
    shards = lax.axis_size("inner")
    same_core = [list(range(core, shards, 2)) for core in range(2)]
    chip = [[j, j + 1] for j in range(0, shards, 2)]
    spread_kv = jnp.broadcast_to(block[None], (shards // 2,) + block.shape)
    half = lax.all_to_all(spread_kv, "inner", 0, 0, axis_index_groups=same_core)
    half = half.reshape(shards // 2 * block.shape[0], 2 * head)
    both = lax.all_to_all(jnp.broadcast_to(half[None], (2,) + half.shape), "inner", 0, 0, axis_index_groups=chip)
    kv = both.reshape(shards * block.shape[0], 2 * head)
    acc_t, peak, total = local_partial(queries, kv)

    normed = (acc_t / total).T
    lse = (peak + jnp.log(total)).reshape(rows)

    ranges = lax.axis_size("outer")
    partners = [[j, j + 1] for j in range(0, ranges, 2)]
    along_z = [list(range(side, ranges, 2)) for side in range(2)]
    normed, lse = merge_step(normed, lse, ranges // 2, along_z)
    normed, lse = merge_step(normed, lse, 2, partners)
    mine = normed.astype(jnp.bfloat16)

    spread = jnp.broadcast_to(mine[None], (2,) + mine.shape)
    pair = lax.all_to_all(spread, "outer", 0, 0, axis_index_groups=partners).reshape(-1, head)
    spread = jnp.broadcast_to(pair[None], (ranges // 2,) + pair.shape)
    return lax.all_to_all(spread, "outer", 0, 0, axis_index_groups=along_z).reshape(rows, head)


def merge_step(normed, lse, members, groups):
    rows, head = normed.shape
    per = rows // members
    tile = -(-3 * per // head)
    tile = -(-tile // 8) * 8
    payload = normed.astype(jnp.bfloat16).reshape(members, per, head)
    parts = jnp.concatenate(split3(lse.reshape(members, per)), axis=1)
    parts = jnp.pad(parts, ((0, 0), (0, tile * head - 3 * per))).reshape(members, tile, head)
    got = lax.all_to_all(jnp.concatenate([payload, parts], axis=1), "outer", 0, 0, axis_index_groups=groups)
    pieces = got[:, per:, :].reshape(members, tile * head)[:, :3 * per].astype(jnp.float32)
    lse_all = pieces[:, :per] + pieces[:, per:2 * per] + pieces[:, 2 * per:]
    joint = jnp.max(lse_all, axis=0)
    weight = jnp.exp(lse_all - joint[None])
    weight_sum = jnp.sum(weight, axis=0)
    summed = jnp.sum(got[:, :per, :].astype(jnp.float32) * weight[:, :, None], axis=0)
    return summed / weight_sum[:, None], joint + jnp.log(weight_sum)


def solution(mesh):
    return jax.shard_map(
        on_device,
        mesh=mesh,
        in_specs=(P("inner", None), P(("outer", "inner"), None), P(("outer", "inner"), None)),
        out_specs=P("inner", None),
        check_vma=False,
    )
```

```python
import functools
import math

import jax
import jax.numpy as jnp
from jax import lax
from jax.experimental import pallas as pl
from jax.experimental.pallas import tpu as pltpu
from jax.sharding import PartitionSpec as P


def attend_kernel(scale, q_ref, k_ref, v_ref, acc_ref, m_ref, l_ref, acc, m_s, l_s):
    step = pl.program_id(1)

    @pl.when(step == 0)
    def _():
        acc[...] = jnp.zeros_like(acc)
        m_s[...] = jnp.full_like(m_s, -1e30)
        l_s[...] = jnp.zeros_like(l_s)

    scores = (
        lax.dot_general(
            k_ref[...], q_ref[...], (((1,), (1,)), ((), ())), preferred_element_type=jnp.float32
        )
        * scale
    )
    m_prev = m_s[...]
    m_new = jnp.maximum(m_prev, jnp.max(scores, axis=0, keepdims=True))
    rescale = jnp.exp(m_prev - m_new)
    probs = jnp.exp(scores - m_new)
    values = jnp.concatenate([v_ref[...], jnp.ones_like(v_ref[...])], axis=1)
    both = lax.dot_general(
        values, probs.astype(jnp.bfloat16), (((0,), (0,)), ((), ())),
        preferred_element_type=jnp.float32,
    )
    head = v_ref.shape[1]
    l_s[...] = l_s[...] * rescale + both[head:head + 1]
    acc[...] = acc[...] * rescale + both[:head]
    m_s[...] = m_new

    @pl.when(step == pl.num_programs(1) - 1)
    def _():
        acc_ref[...] = acc[...]
        m_ref[...] = m_s[...]
        l_ref[...] = l_s[...]


def local_partial(queries, kv, tq=1024, tk=2048):
    tk = math.gcd(kv.shape[0], tk)
    rows, head = queries.shape
    count = kv.shape[0]
    scale = 1.0 / math.sqrt(head)
    grid = (rows // tq, count // tk)
    return pl.pallas_call(
        functools.partial(attend_kernel, scale),
        grid=grid,
        in_specs=[
            pl.BlockSpec((tq, head), lambda i, j: (i, 0)),
            pl.BlockSpec((tk, head), lambda i, j: (j, 0)),
            pl.BlockSpec((tk, head), lambda i, j: (j, 1)),
        ],
        out_specs=[
            pl.BlockSpec((head, tq), lambda i, j: (0, i)),
            pl.BlockSpec((1, tq), lambda i, j: (0, i)),
            pl.BlockSpec((1, tq), lambda i, j: (0, i)),
        ],
        out_shape=[
            jax.ShapeDtypeStruct((head, rows), jnp.float32),
            jax.ShapeDtypeStruct((1, rows), jnp.float32),
            jax.ShapeDtypeStruct((1, rows), jnp.float32),
        ],
        scratch_shapes=[
            pltpu.VMEM((head, tq), jnp.float32),
            pltpu.VMEM((1, tq), jnp.float32),
            pltpu.VMEM((1, tq), jnp.float32),
        ],
        compiler_params=pltpu.CompilerParams(dimension_semantics=("parallel", "arbitrary")),
        cost_estimate=pl.CostEstimate(
            flops=4 * rows * count * head,
            transcendentals=rows * count,
            bytes_accessed=rows * head * 6 + count * head * 4 * grid[0],
        ),
    )(queries, kv, kv)


def split3(x):
    hi = x.astype(jnp.bfloat16)
    rest = x - hi.astype(jnp.float32)
    mid = rest.astype(jnp.bfloat16)
    lo = (rest - mid.astype(jnp.float32)).astype(jnp.bfloat16)
    return hi, mid, lo


def on_device(queries, key_rows, value_rows):
    rows, head = queries.shape
    block = jnp.concatenate([key_rows, value_rows], axis=1)
    shards = lax.axis_size("inner")
    same_core = [list(range(core, shards, 2)) for core in range(2)]
    chip = [[j, j + 1] for j in range(0, shards, 2)]
    spread_kv = jnp.broadcast_to(block[None], (shards // 2,) + block.shape)
    half = lax.all_to_all(spread_kv, "inner", 0, 0, axis_index_groups=same_core)
    half = half.reshape(shards // 2 * block.shape[0], 2 * head)
    both = lax.all_to_all(jnp.broadcast_to(half[None], (2,) + half.shape), "inner", 0, 0, axis_index_groups=chip)
    kv = both.reshape(shards * block.shape[0], 2 * head)
    acc_t, peak, total = local_partial(queries, kv)

    normed = (acc_t / total).T
    lse = (peak + jnp.log(total)).reshape(rows)

    ranges = lax.axis_size("outer")
    me = lax.axis_index("outer")
    partners = [[j, j + 1] for j in range(0, ranges, 2)]
    along_z = [list(range(side, ranges, 2)) for side in range(2)]
    normed, lse = merge_step(normed, lse, 2, partners)
    normed, lse = merge_step(normed, lse, ranges // 2, along_z)
    mine = normed.astype(jnp.bfloat16)

    spread = jnp.broadcast_to(mine[None], (ranges,) + mine.shape)
    got = lax.all_to_all(spread, "outer", 0, 0).reshape(ranges // 2, 2, -1, head)
    return got.transpose(1, 0, 2, 3).reshape(rows, head)


def merge_step(normed, lse, members, groups):
    rows, head = normed.shape
    per = rows // members
    tile = -(-3 * per // head)
    tile = -(-tile // 8) * 8
    payload = normed.astype(jnp.bfloat16).reshape(members, per, head)
    parts = jnp.concatenate(split3(lse.reshape(members, per)), axis=1)
    parts = jnp.pad(parts, ((0, 0), (0, tile * head - 3 * per))).reshape(members, tile, head)
    got = lax.all_to_all(jnp.concatenate([payload, parts], axis=1), "outer", 0, 0, axis_index_groups=groups)
    pieces = got[:, per:, :].reshape(members, tile * head)[:, :3 * per].astype(jnp.float32)
    lse_all = pieces[:, :per] + pieces[:, per:2 * per] + pieces[:, 2 * per:]
    joint = jnp.max(lse_all, axis=0)
    weight = jnp.exp(lse_all - joint[None])
    weight_sum = jnp.sum(weight, axis=0)
    summed = jnp.sum(got[:, :per, :].astype(jnp.float32) * weight[:, :, None], axis=0)
    return summed / weight_sum[:, None], joint + jnp.log(weight_sum)


def solution(mesh):
    return jax.shard_map(
        on_device,
        mesh=mesh,
        in_specs=(P("inner", None), P(("outer", "inner"), None), P(("outer", "inner"), None)),
        out_specs=P("inner", None),
        check_vma=False,
    )
```

```python
import functools
import math

import jax
import jax.numpy as jnp
from jax import lax
from jax.experimental import pallas as pl
from jax.experimental.pallas import tpu as pltpu
from jax.sharding import PartitionSpec as P


def attend_kernel(scale, q_ref, k_ref, v_ref, acc_ref, m_ref, l_ref, acc, m_s, l_s):
    step = pl.program_id(1)

    @pl.when(step == 0)
    def _():
        acc[...] = jnp.zeros_like(acc)
        m_s[...] = jnp.full_like(m_s, -1e30)
        l_s[...] = jnp.zeros_like(l_s)

    scores = (
        lax.dot_general(
            k_ref[...], q_ref[...], (((1,), (1,)), ((), ())), preferred_element_type=jnp.float32
        )
        * scale
    )
    m_prev = m_s[...]
    m_new = jnp.maximum(m_prev, jnp.max(scores, axis=0, keepdims=True))
    rescale = jnp.exp(m_prev - m_new)
    probs = jnp.exp(scores - m_new)
    values = jnp.concatenate([v_ref[...], jnp.ones_like(v_ref[...])], axis=1)
    both = lax.dot_general(
        values, probs.astype(jnp.bfloat16), (((0,), (0,)), ((), ())),
        preferred_element_type=jnp.float32,
    )
    head = v_ref.shape[1]
    l_s[...] = l_s[...] * rescale + both[head:head + 1]
    acc[...] = acc[...] * rescale + both[:head]
    m_s[...] = m_new

    @pl.when(step == pl.num_programs(1) - 1)
    def _():
        acc_ref[...] = acc[...]
        m_ref[...] = m_s[...]
        l_ref[...] = l_s[...]


def local_partial(queries, kv, tq=1024, tk=2048):
    tk = math.gcd(kv.shape[0], tk)
    rows, head = queries.shape
    count = kv.shape[0]
    scale = 1.0 / math.sqrt(head)
    grid = (rows // tq, count // tk)
    return pl.pallas_call(
        functools.partial(attend_kernel, scale),
        grid=grid,
        in_specs=[
            pl.BlockSpec((tq, head), lambda i, j: (i, 0)),
            pl.BlockSpec((tk, head), lambda i, j: (j, 0)),
            pl.BlockSpec((tk, head), lambda i, j: (j, 1)),
        ],
        out_specs=[
            pl.BlockSpec((head, tq), lambda i, j: (0, i)),
            pl.BlockSpec((1, tq), lambda i, j: (0, i)),
            pl.BlockSpec((1, tq), lambda i, j: (0, i)),
        ],
        out_shape=[
            jax.ShapeDtypeStruct((head, rows), jnp.float32),
            jax.ShapeDtypeStruct((1, rows), jnp.float32),
            jax.ShapeDtypeStruct((1, rows), jnp.float32),
        ],
        scratch_shapes=[
            pltpu.VMEM((head, tq), jnp.float32),
            pltpu.VMEM((1, tq), jnp.float32),
            pltpu.VMEM((1, tq), jnp.float32),
        ],
        compiler_params=pltpu.CompilerParams(dimension_semantics=("parallel", "arbitrary")),
        cost_estimate=pl.CostEstimate(
            flops=4 * rows * count * head,
            transcendentals=rows * count,
            bytes_accessed=rows * head * 6 + count * head * 4 * grid[0],
        ),
    )(queries, kv, kv)


def split3(x):
    hi = x.astype(jnp.bfloat16)
    rest = x - hi.astype(jnp.float32)
    mid = rest.astype(jnp.bfloat16)
    lo = (rest - mid.astype(jnp.float32)).astype(jnp.bfloat16)
    return hi, mid, lo


def on_device(queries, key_rows, value_rows):
    rows, head = queries.shape
    block = jnp.concatenate([key_rows, value_rows], axis=1)
    shards = lax.axis_size("inner")
    ys = 4
    xs = shards // (2 * ys)
    along_y = [[(x * ys + y) * 2 + core for y in range(ys)] for x in range(xs) for core in range(2)]
    along_x = [[(x * ys + y) * 2 + core for x in range(xs)] for y in range(ys) for core in range(2)]
    chip = [[j, j + 1] for j in range(0, shards, 2)]
    spread_kv = jnp.broadcast_to(block[None], (ys,) + block.shape)
    half = lax.all_to_all(spread_kv, "inner", 0, 0, axis_index_groups=along_y)
    half = half.reshape(ys * block.shape[0], 2 * head)
    half = lax.all_to_all(jnp.broadcast_to(half[None], (xs,) + half.shape), "inner", 0, 0, axis_index_groups=along_x)
    half = half.reshape(shards // 2 * block.shape[0], 2 * head)
    both = lax.all_to_all(jnp.broadcast_to(half[None], (2,) + half.shape), "inner", 0, 0, axis_index_groups=chip)
    kv = both.reshape(shards * block.shape[0], 2 * head)
    acc_t, peak, total = local_partial(queries, kv)

    normed = (acc_t / total).T
    lse = (peak + jnp.log(total)).reshape(rows)

    ranges = lax.axis_size("outer")
    partners = [[j, j + 1] for j in range(0, ranges, 2)]
    along_z = [list(range(side, ranges, 2)) for side in range(2)]
    normed, lse = merge_step(normed, lse, 2, partners)
    normed, lse = merge_step(normed, lse, ranges // 2, along_z)
    mine = normed.astype(jnp.bfloat16)

    spread = jnp.broadcast_to(mine[None], (ranges,) + mine.shape)
    got = lax.all_to_all(spread, "outer", 0, 0).reshape(ranges // 2, 2, -1, head)
    return got.transpose(1, 0, 2, 3).reshape(rows, head)


def merge_step(normed, lse, members, groups):
    rows, head = normed.shape
    per = rows // members
    tile = -(-3 * per // head)
    tile = -(-tile // 8) * 8
    payload = normed.astype(jnp.bfloat16).reshape(members, per, head)
    parts = jnp.concatenate(split3(lse.reshape(members, per)), axis=1)
    parts = jnp.pad(parts, ((0, 0), (0, tile * head - 3 * per))).reshape(members, tile, head)
    got = lax.all_to_all(jnp.concatenate([payload, parts], axis=1), "outer", 0, 0, axis_index_groups=groups)
    pieces = got[:, per:, :].reshape(members, tile * head)[:, :3 * per].astype(jnp.float32)
    lse_all = pieces[:, :per] + pieces[:, per:2 * per] + pieces[:, 2 * per:]
    joint = jnp.max(lse_all, axis=0)
    weight = jnp.exp(lse_all - joint[None])
    weight_sum = jnp.sum(weight, axis=0)
    summed = jnp.sum(got[:, :per, :].astype(jnp.float32) * weight[:, :, None], axis=0)
    return summed / weight_sum[:, None], joint + jnp.log(weight_sum)


def solution(mesh):
    return jax.shard_map(
        on_device,
        mesh=mesh,
        in_specs=(P("inner", None), P(("outer", "inner"), None), P(("outer", "inner"), None)),
        out_specs=P("inner", None),
        check_vma=False,
    )
```

```python
import functools
import math

import jax
import jax.numpy as jnp
from jax import lax
from jax.experimental import pallas as pl
from jax.experimental.pallas import tpu as pltpu
from jax.sharding import PartitionSpec as P


def attend_kernel(scale, q_ref, k_ref, v_ref, acc_ref, m_ref, l_ref, acc, m_s, l_s):
    step = pl.program_id(1)

    @pl.when(step == 0)
    def _():
        acc[...] = jnp.zeros_like(acc)
        m_s[...] = jnp.full_like(m_s, -1e30)
        l_s[...] = jnp.zeros_like(l_s)

    scores = (
        lax.dot_general(
            k_ref[...], q_ref[...], (((1,), (1,)), ((), ())), preferred_element_type=jnp.float32
        )
        * scale
    )
    m_prev = m_s[...]
    m_new = jnp.maximum(m_prev, jnp.max(scores, axis=0, keepdims=True))
    rescale = jnp.exp(m_prev - m_new)
    probs = jnp.exp(scores - m_new)
    values = jnp.concatenate([v_ref[...], jnp.ones_like(v_ref[...])], axis=1)
    both = lax.dot_general(
        values, probs.astype(jnp.bfloat16), (((0,), (0,)), ((), ())),
        preferred_element_type=jnp.float32,
    )
    head = v_ref.shape[1]
    l_s[...] = l_s[...] * rescale + both[head:head + 1]
    acc[...] = acc[...] * rescale + both[:head]
    m_s[...] = m_new

    @pl.when(step == pl.num_programs(1) - 1)
    def _():
        acc_ref[...] = acc[...]
        m_ref[...] = m_s[...]
        l_ref[...] = l_s[...]


def local_partial(queries, kv, tq=1024, tk=4096):
    tk = math.gcd(kv.shape[0], tk)
    rows, head = queries.shape
    count = kv.shape[0]
    scale = 1.0 / math.sqrt(head)
    grid = (rows // tq, count // tk)
    return pl.pallas_call(
        functools.partial(attend_kernel, scale),
        grid=grid,
        in_specs=[
            pl.BlockSpec((tq, head), lambda i, j: (i, 0)),
            pl.BlockSpec((tk, head), lambda i, j: (j, 0)),
            pl.BlockSpec((tk, head), lambda i, j: (j, 1)),
        ],
        out_specs=[
            pl.BlockSpec((head, tq), lambda i, j: (0, i)),
            pl.BlockSpec((1, tq), lambda i, j: (0, i)),
            pl.BlockSpec((1, tq), lambda i, j: (0, i)),
        ],
        out_shape=[
            jax.ShapeDtypeStruct((head, rows), jnp.float32),
            jax.ShapeDtypeStruct((1, rows), jnp.float32),
            jax.ShapeDtypeStruct((1, rows), jnp.float32),
        ],
        scratch_shapes=[
            pltpu.VMEM((head, tq), jnp.float32),
            pltpu.VMEM((1, tq), jnp.float32),
            pltpu.VMEM((1, tq), jnp.float32),
        ],
        compiler_params=pltpu.CompilerParams(dimension_semantics=("parallel", "arbitrary")),
        cost_estimate=pl.CostEstimate(
            flops=4 * rows * count * head,
            transcendentals=rows * count,
            bytes_accessed=rows * head * 6 + count * head * 4 * grid[0],
        ),
    )(queries, kv, kv)


def split3(x):
    hi = x.astype(jnp.bfloat16)
    rest = x - hi.astype(jnp.float32)
    mid = rest.astype(jnp.bfloat16)
    lo = (rest - mid.astype(jnp.float32)).astype(jnp.bfloat16)
    return hi, mid, lo


def on_device(queries, key_rows, value_rows):
    rows, head = queries.shape
    block = jnp.concatenate([key_rows, value_rows], axis=1)
    shards = lax.axis_size("inner")
    same_core = [list(range(core, shards, 2)) for core in range(2)]
    chip = [[j, j + 1] for j in range(0, shards, 2)]
    spread_kv = jnp.broadcast_to(block[None], (shards // 2,) + block.shape)
    half = lax.all_to_all(spread_kv, "inner", 0, 0, axis_index_groups=same_core)
    half = half.reshape(shards // 2 * block.shape[0], 2 * head)
    both = lax.all_to_all(jnp.broadcast_to(half[None], (2,) + half.shape), "inner", 0, 0, axis_index_groups=chip)
    kv = both.reshape(shards * block.shape[0], 2 * head)
    acc_t, peak, total = local_partial(queries, kv)

    normed = (acc_t / total).T
    lse = (peak + jnp.log(total)).reshape(rows)

    ranges = lax.axis_size("outer")
    me = lax.axis_index("outer")
    partners = [[j, j + 1] for j in range(0, ranges, 2)]
    along_z = [list(range(side, ranges, 2)) for side in range(2)]
    normed, lse = merge_step(normed, lse, 2, partners)
    normed, lse = merge_step(normed, lse, ranges // 2, along_z)
    mine = normed.astype(jnp.bfloat16)

    spread = jnp.broadcast_to(mine[None], (ranges,) + mine.shape)
    got = lax.all_to_all(spread, "outer", 0, 0).reshape(ranges // 2, 2, -1, head)
    return got.transpose(1, 0, 2, 3).reshape(rows, head)


def merge_step(normed, lse, members, groups):
    rows, head = normed.shape
    per = rows // members
    tile = -(-3 * per // head)
    tile = -(-tile // 8) * 8
    payload = normed.astype(jnp.bfloat16).reshape(members, per, head)
    parts = jnp.concatenate(split3(lse.reshape(members, per)), axis=1)
    parts = jnp.pad(parts, ((0, 0), (0, tile * head - 3 * per))).reshape(members, tile, head)
    got = lax.all_to_all(jnp.concatenate([payload, parts], axis=1), "outer", 0, 0, axis_index_groups=groups)
    pieces = got[:, per:, :].reshape(members, tile * head)[:, :3 * per].astype(jnp.float32)
    lse_all = pieces[:, :per] + pieces[:, per:2 * per] + pieces[:, 2 * per:]
    joint = jnp.max(lse_all, axis=0)
    weight = jnp.exp(lse_all - joint[None])
    weight_sum = jnp.sum(weight, axis=0)
    summed = jnp.sum(got[:, :per, :].astype(jnp.float32) * weight[:, :, None], axis=0)
    return summed / weight_sum[:, None], joint + jnp.log(weight_sum)


def solution(mesh):
    return jax.shard_map(
        on_device,
        mesh=mesh,
        in_specs=(P("inner", None), P(("outer", "inner"), None), P(("outer", "inner"), None)),
        out_specs=P("inner", None),
        check_vma=False,
    )
```
